256 devices in a mesh: leaf: 64 (over y, z, core), layer: 4 (over x).
Axes of the slice: x: 4, y: 4, z: 8, core: 2. Of those that a mesh axis runs over, the one named last changes fastest.
Arguments:
- schur_blocks: float32 [64, 2048, 2048], P('leaf', 'layer'), as said below
Outputs:
- merged: float32 [64, 1536, 3072], P('leaf', 'layer')
- cousin_sum: float32 [64, 512, 512], P('leaf', 'layer')
Inputs may be any that keep to these rules, and one draw needn't show every extreme that they name: `schur_blocks`: symmetric and positive definite.
All inputs are finite; a program needn't handle non-finite values.
Results may differ from the reference program's by a relative error of at most 0.0001.
Values sent between devices are 32-bit elements; how exact they have to be, the bound alone decides.
No kernel may reach another device: no remote copies, remote signals or barrier semaphores. Data moves between devices by JAX's collectives and lax.ppermute only.
A program may use at most 64 MiB of HBM per device.

```python
import math
import jax
import jax.numpy as jnp
import numpy as np
from jax import lax

IFACE = 2048
SHARED = 512
LEAVES = 64
PS = 128
OUTER = 1536
OS = 384
SHS = 128
N_LAYER = 4


def draw_schur_blocks(key, part):
    neighbours = 64.0
    reach = (neighbours / (2.0 * math.pi * IFACE)) ** 0.5
    strength = 24.0 / neighbours
    spread = 0.3

    def one_leaf(leaf_index):
        leaf_key = jax.random.fold_in(key, leaf_index)
        place_key = jax.random.fold_in(leaf_key, 21)
        noise_key = jax.random.fold_in(leaf_key, 22)
        shift_key = jax.random.fold_in(leaf_key, 23)
        places = jax.random.uniform(place_key, (IFACE, 2), jnp.float32)
        delta_x = places[:, None, 0] - places[None, :, 0]
        delta_y = places[:, None, 1] - places[None, :, 1]
        distance = jnp.sqrt(delta_x * delta_x + delta_y * delta_y)
        kernel = strength * jnp.exp(-distance / reach)
        rough = jnp.clip(jax.random.normal(noise_key, (IFACE, IFACE), jnp.float32), -6.0, 6.0)
        rough = rough * (spread / (2.0 * IFACE) ** 0.5)
        symmetric = rough + rough.T
        eye_mask = jnp.eye(IFACE, dtype=jnp.float32)
        shift = jax.random.uniform(shift_key, (IFACE,), jnp.float32, 1.0, 2.0)
        matrix = kernel + symmetric * (1.0 - eye_mask) + shift[:, None] * eye_mask
        return matrix
    return lax.map(one_leaf, jnp.arange(LEAVES, dtype=jnp.int32))


def setup_inputs(seed: int = 0) -> dict:
    streams_of = jax.random.split(jax.random.key(seed), 2)
    return {
        "schur_blocks": draw_schur_blocks(jax.random.fold_in(streams_of[1], 71), 0),
    }


def index_lists():
    slab = IFACE // N_LAYER
    sep_rows = np.array([g * slab + j for g in range(N_LAYER) for j in range(PS)], dtype=np.int32)
    out_rows = np.array([g * slab + j for g in range(N_LAYER) for j in range(PS, slab)], dtype=np.int32)
    shared_pos = np.array([g * OS + j for g in range(N_LAYER) for j in range(SHS)], dtype=np.int32)
    return (sep_rows, out_rows, shared_pos)

def reference(schur_blocks):
    sep_rows, out_rows, shared_pos = index_lists()
    highest = lax.Precision.HIGHEST

    def condense(pair):
        first = pair[0]
        second = pair[1]
        sepmat = first[sep_rows][:, sep_rows] + second[sep_rows][:, sep_rows]
        lower = jnp.linalg.cholesky(sepmat)
        factors = []
        for member in (first, second):
            coupling = member[out_rows][:, sep_rows]
            factors.append(lax.linalg.triangular_solve(lower, coupling.T, left_side=True, lower=True))
        joined = jnp.concatenate(factors, axis=1)
        blocks = []
        zeros_block = jnp.zeros((OUTER, OUTER), jnp.float32)
        for member_idx, member in enumerate((first, second)):
            direct = member[out_rows][:, out_rows]
            parts = [direct, zeros_block] if member_idx == 0 else [zeros_block, direct]
            product = jnp.dot(factors[member_idx].T.astype(jnp.float32), joined.astype(jnp.float32), precision=highest, preferred_element_type=jnp.float32)
            blocks.append(jnp.concatenate(parts, axis=1) - product)
        return jnp.stack(blocks)
    pairs = schur_blocks.reshape(LEAVES // 2, 2, IFACE, IFACE)
    merged = lax.map(condense, pairs).reshape(LEAVES, OUTER, 2 * OUTER)
    grouped = merged.reshape(LEAVES // 2, 2, OUTER, 2, OUTER)
    own_block = jnp.stack([grouped[:, 0, :, 0, :], grouped[:, 1, :, 1, :]], axis=1).reshape(LEAVES, OUTER, OUTER)
    picked = own_block[:, shared_pos][:, :, shared_pos]
    quads = picked.reshape(LEAVES // 4, 2, 2, SHARED, SHARED)
    cousin_sum = (quads + quads[:, ::-1]).reshape(LEAVES, SHARED, SHARED)
    return (merged, cousin_sum)
```

```python
import jax
import jax.numpy as jnp
from jax import lax
from jax.sharding import PartitionSpec as P

SEP = 512
SHARED = 512
BLOCK = 128
HIGHEST = lax.Precision.HIGHEST


def partner(value, axis, stride):
    mask = 2**stride
    pairs = [(source, source ^ mask) for source in range(lax.axis_size(axis))]
    return lax.ppermute(value, axis, pairs)


def gather_layer(value):
    layers = lax.axis_size("layer")
    rows = value.shape[0]
    me = lax.axis_index("layer")
    pieces = [value]
    for shift in range(1, layers):
        pairs = [((dest + shift) % layers, dest) for dest in range(layers)]
        pieces.append(lax.ppermute(value, "layer", pairs))
    doubled = jnp.concatenate(pieces + pieces, axis=0)
    start = ((layers - me) % layers) * rows
    return lax.dynamic_slice_in_dim(doubled, start, layers * rows, axis=0)


def mm(a, b):
    return jnp.dot(a, b, precision=HIGHEST, preferred_element_type=jnp.float32)


def mm_nt(a, b):
    return lax.dot_general(
        a, b, (((1,), (1,)), ((), ())), precision=HIGHEST, preferred_element_type=jnp.float32
    )


def blocked_cholesky(sepmat):
    n = sepmat.shape[0]
    nb = n // BLOCK
    eye = jnp.eye(BLOCK, dtype=jnp.float32)
    trailing = sepmat
    panels = []
    inverses = []
    for k in range(nb):
        diag = trailing[:BLOCK, :BLOCK]
        lkk = jnp.linalg.cholesky(diag)
        inv = lax.linalg.triangular_solve(lkk, eye, left_side=True, lower=True)
        inverses.append(inv)
        if k + 1 < nb:
            below = trailing[BLOCK:, :BLOCK]
            panel = mm_nt(below, inv)
            panels.append(panel)
            trailing = trailing[BLOCK:, BLOCK:] - mm_nt(panel, panel)
    return panels, inverses


def forward_solve(panels, inverses, rhs):
    nb = len(inverses)
    out = []
    rest = rhs
    for k in range(nb):
        gk = mm(inverses[k], rest[:BLOCK])
        out.append(gk)
        if k + 1 < nb:
            rest = rest[BLOCK:] - mm(panels[k], gk)
    return jnp.concatenate(out, axis=0)


def on_device(schur_blocks):
    layers = lax.axis_size("layer")
    local = schur_blocks[0]
    slab = local.shape[0]
    sep_slab = SEP // layers
    outer_slab = slab - sep_slab
    shared_slab = SHARED // layers
    outer_all = local.shape[1] - SEP
    me = lax.axis_index("layer")
    parity = lax.axis_index("leaf") % 2

    sep_rows = local[:sep_slab]
    sep_cols = jnp.concatenate(
        [sep_rows[:, h * slab : h * slab + sep_slab] for h in range(layers)], axis=1
    )
    out_cols = jnp.concatenate(
        [sep_rows[:, h * slab + sep_slab : (h + 1) * slab] for h in range(layers)], axis=1
    )
    sibling = partner(sep_cols, "leaf", 0)
    sepmat = gather_layer(sep_cols + sibling)

    coupling_t = gather_layer(out_cols)
    coupling_sib = partner(coupling_t, "leaf", 0)
    rhs = jnp.where(
        parity == 0,
        jnp.concatenate([coupling_t, coupling_sib], axis=1),
        jnp.concatenate([coupling_sib, coupling_t], axis=1),
    )

    panels, inverses = blocked_cholesky(sepmat)
    joined = forward_solve(panels, inverses, rhs)
    factor_own = lax.dynamic_slice_in_dim(
        joined, parity * outer_all + me * outer_slab, outer_slab, axis=1
    )

    direct_rows = jnp.concatenate(
        [local[sep_slab:, h * slab + sep_slab : (h + 1) * slab] for h in range(layers)], axis=1
    )
    selector = (jnp.arange(2) == parity).astype(jnp.float32)
    product = lax.dot_general(
        factor_own, joined, (((0,), (0,)), ((), ())), precision=HIGHEST,
        preferred_element_type=jnp.float32,
    ).reshape(outer_slab, 2, outer_all)
    merged_rows = direct_rows[:, None, :] * selector[None, :, None] - product
    merged = merged_rows.reshape(outer_slab, 2 * outer_all)
    grouped = merged_rows.reshape(outer_slab, 2, layers, outer_slab)[:shared_slab]
    own_block = jnp.where(parity == 0, grouped[:, 0], grouped[:, 1])
    own_shared = own_block[:, :, :shared_slab].reshape(shared_slab, SHARED)
    cousin = partner(own_shared, "leaf", 1)
    cousin_sum = own_shared + cousin
    return (merged[None], cousin_sum[None])


def solution(mesh):
    placed = (P("leaf", "layer", None),)
    return jax.shard_map(
        on_device,
        mesh=mesh,
        in_specs=placed,
        out_specs=(P("leaf", "layer", None), P("leaf", "layer", None)),
        check_vma=False,
    )
```

```python
import jax
import jax.numpy as jnp
from jax import lax
from jax.sharding import PartitionSpec as P

SEP = 512
SHARED = 512
BLOCK = 128
HIGHEST = lax.Precision.HIGHEST


def partner(value, axis, stride):
    mask = 2**stride
    pairs = [(source, source ^ mask) for source in range(lax.axis_size(axis))]
    return lax.ppermute(value, axis, pairs)


def gather_layer(value):
    layers = lax.axis_size("layer")
    pieces = [value]
    for shift in range(1, layers):
        pairs = [((dest + shift) % layers, dest) for dest in range(layers)]
        pieces.append(lax.ppermute(value, "layer", pairs))
    return jnp.concatenate(pieces, axis=0)


def mm(a, b):
    return jnp.dot(a, b, precision=HIGHEST, preferred_element_type=jnp.float32)


def mm_nt(a, b):
    return lax.dot_general(
        a, b, (((1,), (1,)), ((), ())), precision=HIGHEST, preferred_element_type=jnp.float32
    )


def blocked_cholesky(sepmat):
    n = sepmat.shape[0]
    nb = n // BLOCK
    eye = jnp.eye(BLOCK, dtype=jnp.float32)
    trailing = sepmat
    panels = []
    inverses = []
    for k in range(nb):
        diag = trailing[:BLOCK, :BLOCK]
        lkk = jnp.linalg.cholesky(diag)
        inv = lax.linalg.triangular_solve(lkk, eye, left_side=True, lower=True)
        inverses.append(inv)
        if k + 1 < nb:
            below = trailing[BLOCK:, :BLOCK]
            panel = mm_nt(below, inv)
            panels.append(panel)
            trailing = trailing[BLOCK:, BLOCK:] - mm_nt(panel, panel)
    return panels, inverses


def forward_solve(panels, inverses, rhs):
    nb = len(inverses)
    out = []
    rest = rhs
    for k in range(nb):
        gk = mm(inverses[k], rest[:BLOCK])
        out.append(gk)
        if k + 1 < nb:
            rest = rest[BLOCK:] - mm(panels[k], gk)
    return jnp.concatenate(out, axis=0)


def on_device(schur_blocks):
    layers = lax.axis_size("layer")
    local = schur_blocks[0]
    slab = local.shape[0]
    sep_slab = SEP // layers
    outer_slab = slab - sep_slab
    shared_slab = SHARED // layers
    outer_all = local.shape[1] - SEP
    me = lax.axis_index("layer")
    parity = lax.axis_index("leaf") % 2

    sep_rows = local[:sep_slab]
    sep_cols = jnp.concatenate(
        [sep_rows[:, h * slab : h * slab + sep_slab] for h in range(layers)], axis=1
    )
    out_cols = jnp.concatenate(
        [sep_rows[:, h * slab + sep_slab : (h + 1) * slab] for h in range(layers)], axis=1
    )
    sibling = partner(sep_cols, "leaf", 0)
    rows_rel = gather_layer(sep_cols + sibling)
    doubled = jnp.concatenate([rows_rel, rows_rel], axis=1)
    sepmat = lax.dynamic_slice_in_dim(doubled, me * sep_slab, SEP, axis=1)

    out_cols, sepmat = lax.optimization_barrier((out_cols, sepmat))
    coupling_own = gather_layer(out_cols)
    coupling_sib = partner(coupling_own, "leaf", 0)

    panels, inverses = blocked_cholesky(sepmat)
    joined = forward_solve(panels, inverses, jnp.concatenate([coupling_own, coupling_sib], axis=1))
    factor_own = lax.dynamic_slice_in_dim(joined, me * outer_slab, outer_slab, axis=1)

    direct_rows = jnp.concatenate(
        [local[sep_slab:, h * slab + sep_slab : (h + 1) * slab] for h in range(layers)], axis=1
    )
    product = lax.dot_general(
        factor_own, joined, (((0,), (0,)), ((), ())), precision=HIGHEST,
        preferred_element_type=jnp.float32,
    )
    with_own = direct_rows - product[:, :outer_all]
    with_sib = -product[:, outer_all:]
    merged = jnp.where(
        parity == 0,
        jnp.concatenate([with_own, with_sib], axis=1),
        jnp.concatenate([with_sib, with_own], axis=1),
    )
    own_shared = jnp.concatenate(
        [with_own[:shared_slab, h * outer_slab : h * outer_slab + shared_slab] for h in range(layers)],
        axis=1,
    )
    cousin = partner(own_shared, "leaf", 1)
    cousin_sum = own_shared + cousin
    return (merged[None], cousin_sum[None])


def solution(mesh):
    placed = (P("leaf", "layer", None),)
    return jax.shard_map(
        on_device,
        mesh=mesh,
        in_specs=placed,
        out_specs=(P("leaf", "layer", None), P("leaf", "layer", None)),
        check_vma=False,
    )
```

```python
import jax
import jax.numpy as jnp
from jax import lax
from jax.experimental import pallas as pl
from jax.experimental.pallas import tpu as pltpu
from jax.sharding import PartitionSpec as P

SEP = 512
SHARED = 512
BLOCK = 128
HIGHEST = lax.Precision.HIGHEST


def partner(value, axis, stride):
    mask = 2**stride
    pairs = [(source, source ^ mask) for source in range(lax.axis_size(axis))]
    return lax.ppermute(value, axis, pairs)


def gather_layer(value):
    layers = lax.axis_size("layer")
    pieces = [value]
    for shift in range(1, layers):
        pairs = [((dest + shift) % layers, dest) for dest in range(layers)]
        pieces.append(lax.ppermute(value, "layer", pairs))
    return jnp.concatenate(pieces, axis=0)


def _inv_factor_kernel(a_ref, x_ref, s_ref, w_ref):
    n = a_ref.shape[0]
    s_ref[...] = a_ref[...]
    rows_i = lax.broadcasted_iota(jnp.int32, (n, n), 0)
    cols_i = lax.broadcasted_iota(jnp.int32, (n, n), 1)
    w_ref[...] = jnp.where(rows_i == cols_i, 1.0, 0.0).astype(jnp.float32)
    x_ref[...] = jnp.zeros((n, n), jnp.float32)
    lane = lax.broadcasted_iota(jnp.int32, (1, n), 1)
    for grp in range(n // 8):
        r0 = grp * 8
        span = n - r0
        row_id = lax.broadcasted_iota(jnp.int32, (span, 1), 0) + r0

        def step(i, carry, r0=r0, span=span, row_id=row_id):
            j = r0 + i
            row_j = s_ref[pl.ds(j, 1), :]
            d = jnp.sum(jnp.where(lane == j, row_j, 0.0), axis=1, keepdims=True)
            scale = 1.0 / jnp.sqrt(d)
            l_row = jnp.where(lane >= j, row_j * scale, 0.0)
            x_row = w_ref[pl.ds(j, 1), :] * scale
            x_ref[pl.ds(j, 1), :] = x_row
            rows = s_ref[r0:, :]
            col = jnp.sum(jnp.where(lane == j, rows, 0.0), axis=1, keepdims=True)
            l_col = jnp.where(row_id > j, col * scale, 0.0)
            s_ref[r0:, :] = rows - l_col * l_row
            w_ref[r0:, :] = w_ref[r0:, :] - l_col * x_row
            return carry

        lax.fori_loop(0, 8, step, 0)


def inverse_factor(a):
    n = a.shape[0]
    return pl.pallas_call(
        _inv_factor_kernel,
        out_shape=jax.ShapeDtypeStruct((n, n), jnp.float32),
        in_specs=[pl.BlockSpec(memory_space=pltpu.VMEM)],
        out_specs=pl.BlockSpec(memory_space=pltpu.VMEM),
        scratch_shapes=[pltpu.VMEM((n, n), jnp.float32), pltpu.VMEM((n, n), jnp.float32)],
    )(a)


def mm(a, b):
    return jnp.dot(a, b, precision=HIGHEST, preferred_element_type=jnp.float32)


def mm_nt(a, b):
    return lax.dot_general(
        a, b, (((1,), (1,)), ((), ())), precision=HIGHEST, preferred_element_type=jnp.float32
    )


def blocked_cholesky(sepmat):
    n = sepmat.shape[0]
    nb = n // BLOCK
    trailing = sepmat
    panels = []
    inverses = []
    for k in range(nb):
        diag = trailing[:BLOCK, :BLOCK]
        inv = inverse_factor(diag)
        inverses.append(inv)
        if k + 1 < nb:
            below = trailing[BLOCK:, :BLOCK]
            panel = mm_nt(below, inv)
            panels.append(panel)
            trailing = trailing[BLOCK:, BLOCK:] - mm_nt(panel, panel)
    return panels, inverses


def forward_solve(panels, inverses, rhs):
    nb = len(inverses)
    out = []
    rest = rhs
    for k in range(nb):
        gk = mm(inverses[k], rest[:BLOCK])
        out.append(gk)
        if k + 1 < nb:
            rest = rest[BLOCK:] - mm(panels[k], gk)
    return jnp.concatenate(out, axis=0)


def on_device(schur_blocks):
    layers = lax.axis_size("layer")
    local = schur_blocks[0]
    slab = local.shape[0]
    sep_slab = SEP // layers
    outer_slab = slab - sep_slab
    shared_slab = SHARED // layers
    outer_all = local.shape[1] - SEP
    me = lax.axis_index("layer")
    parity = lax.axis_index("leaf") % 2

    sep_rows = local[:sep_slab]
    sep_cols = jnp.concatenate(
        [sep_rows[:, h * slab : h * slab + sep_slab] for h in range(layers)], axis=1
    )
    out_cols = jnp.concatenate(
        [sep_rows[:, h * slab + sep_slab : (h + 1) * slab] for h in range(layers)], axis=1
    )
    sibling = partner(sep_cols, "leaf", 0)
    rows_rel = gather_layer(sep_cols + sibling)
    doubled = jnp.concatenate([rows_rel, rows_rel], axis=1)
    sepmat = lax.dynamic_slice_in_dim(doubled, me * sep_slab, SEP, axis=1)

    out_cols, sepmat = lax.optimization_barrier((out_cols, sepmat))
    coupling_own = gather_layer(out_cols)
    coupling_sib = partner(coupling_own, "leaf", 0)

    panels, inverses = blocked_cholesky(sepmat)
    joined = forward_solve(panels, inverses, jnp.concatenate([coupling_own, coupling_sib], axis=1))
    factor_own = lax.dynamic_slice_in_dim(joined, me * outer_slab, outer_slab, axis=1)

    direct_rows = jnp.concatenate(
        [local[sep_slab:, h * slab + sep_slab : (h + 1) * slab] for h in range(layers)], axis=1
    )
    product = lax.dot_general(
        factor_own, joined, (((0,), (0,)), ((), ())), precision=HIGHEST,
        preferred_element_type=jnp.float32,
    )
    with_own = direct_rows - product[:, :outer_all]
    with_sib = -product[:, outer_all:]
    merged = jnp.where(
        parity == 0,
        jnp.concatenate([with_own, with_sib], axis=1),
        jnp.concatenate([with_sib, with_own], axis=1),
    )
    own_shared = jnp.concatenate(
        [with_own[:shared_slab, h * outer_slab : h * outer_slab + shared_slab] for h in range(layers)],
        axis=1,
    )
    cousin = partner(own_shared, "leaf", 1)
    cousin_sum = own_shared + cousin
    return (merged[None], cousin_sum[None])


def solution(mesh):
    placed = (P("leaf", "layer", None),)
    return jax.shard_map(
        on_device,
        mesh=mesh,
        in_specs=placed,
        out_specs=(P("leaf", "layer", None), P("leaf", "layer", None)),
        check_vma=False,
    )
```

```python
import jax
import jax.numpy as jnp
from jax import lax
from jax.experimental import pallas as pl
from jax.experimental.pallas import tpu as pltpu
from jax.sharding import PartitionSpec as P


SEP = 512
SHARED = 512
BLOCK = 128
HIGHEST = lax.Precision.HIGHEST


def partner(value, axis, stride):
    mask = 2**stride
    pairs = [(source, source ^ mask) for source in range(lax.axis_size(axis))]
    return lax.ppermute(value, axis, pairs)


def gather_layer(value):
    layers = lax.axis_size("layer")
    pieces = [value]
    for shift in range(1, layers):
        pairs = [((dest + shift) % layers, dest) for dest in range(layers)]
        pieces.append(lax.ppermute(value, "layer", pairs))
    return jnp.concatenate(pieces, axis=0)


def _inv_factor_kernel(a_ref, x_ref, s_ref, w_ref):
    n = a_ref.shape[0]
    s_ref[...] = a_ref[...]
    rows_i = lax.broadcasted_iota(jnp.int32, (n, n), 0)
    cols_i = lax.broadcasted_iota(jnp.int32, (n, n), 1)
    w_ref[...] = jnp.where(rows_i == cols_i, 1.0, 0.0).astype(jnp.float32)
    x_ref[...] = jnp.zeros((n, n), jnp.float32)
    lane = lax.broadcasted_iota(jnp.int32, (1, n), 1)
    for grp in range(n // 8):
        r0 = grp * 8
        span = n - r0
        row_id = lax.broadcasted_iota(jnp.int32, (span, 1), 0) + r0

        def step(i, carry, r0=r0, span=span, row_id=row_id):
            j = r0 + i
            row_j = s_ref[pl.ds(j, 1), :]
            d = jnp.sum(jnp.where(lane == j, row_j, 0.0), axis=1, keepdims=True)
            scale = 1.0 / jnp.sqrt(d)
            l_row = jnp.where(lane >= j, row_j * scale, 0.0)
            x_row = w_ref[pl.ds(j, 1), :] * scale
            x_ref[pl.ds(j, 1), :] = x_row
            rows = s_ref[r0:, :]
            col = jnp.sum(jnp.where(lane == j, rows, 0.0), axis=1, keepdims=True)
            l_col = jnp.where(row_id > j, col * scale, 0.0)
            s_ref[r0:, :] = rows - l_col * l_row
            w_ref[r0:, :] = w_ref[r0:, :] - l_col * x_row
            return carry

        lax.fori_loop(0, 8, step, 0)


def inverse_factor(a):
    n = a.shape[0]
    return pl.pallas_call(
        _inv_factor_kernel,
        out_shape=jax.ShapeDtypeStruct((n, n), jnp.float32),
        in_specs=[pl.BlockSpec(memory_space=pltpu.VMEM)],
        out_specs=pl.BlockSpec(memory_space=pltpu.VMEM),
        scratch_shapes=[pltpu.VMEM((n, n), jnp.float32), pltpu.VMEM((n, n), jnp.float32)],
    )(a)


def mm(a, b):
    return jnp.dot(a, b, precision=HIGHEST, preferred_element_type=jnp.float32)


def mm_nt(a, b):
    return lax.dot_general(
        a, b, (((1,), (1,)), ((), ())), precision=HIGHEST, preferred_element_type=jnp.float32
    )


def blocked_cholesky(sepmat):
    n = sepmat.shape[0]
    nb = n // BLOCK
    trailing = sepmat
    panels = []
    inverses = []
    for k in range(nb):
        diag = trailing[:BLOCK, :BLOCK]
        inv = inverse_factor(diag)
        inverses.append(inv)
        if k + 1 < nb:
            below = trailing[BLOCK:, :BLOCK]
            panel = mm_nt(below, inv)
            panels.append(panel)
            trailing = trailing[BLOCK:, BLOCK:] - mm_nt(panel, panel)
    return panels, inverses


def forward_solve(panels, inverses, rhs):
    nb = len(inverses)
    out = []
    rest = rhs
    for k in range(nb):
        gk = mm(inverses[k], rest[:BLOCK])
        out.append(gk)
        if k + 1 < nb:
            rest = rest[BLOCK:] - mm(panels[k], gk)
    return jnp.concatenate(out, axis=0)


def condense(schur_blocks):
    layers = lax.axis_size("layer")
    local = schur_blocks[0]
    slab = local.shape[0]
    sep_slab = SEP // layers
    outer_slab = slab - sep_slab
    shared_slab = SHARED // layers
    outer_all = local.shape[1] - SEP
    me = lax.axis_index("layer")
    parity = lax.axis_index("leaf") % 2

    sep_rows = local[:sep_slab]
    sep_cols = jnp.concatenate(
        [sep_rows[:, h * slab : h * slab + sep_slab] for h in range(layers)], axis=1
    )
    out_cols = jnp.concatenate(
        [sep_rows[:, h * slab + sep_slab : (h + 1) * slab] for h in range(layers)], axis=1
    )
    sibling = partner(sep_cols, "leaf", 0)
    rows_rel = gather_layer(sep_cols + sibling)
    doubled = jnp.concatenate([rows_rel, rows_rel], axis=1)
    sepmat = lax.dynamic_slice_in_dim(doubled, me * sep_slab, SEP, axis=1)

    out_cols, sepmat = lax.optimization_barrier((out_cols, sepmat))
    coupling_own = gather_layer(out_cols)
    coupling_sib = partner(coupling_own, "leaf", 0)

    panels, inverses = blocked_cholesky(sepmat)
    joined = forward_solve(panels, inverses, jnp.concatenate([coupling_own, coupling_sib], axis=1))
    factor_own = lax.dynamic_slice_in_dim(joined, me * outer_slab, outer_slab, axis=1)

    direct_rows = jnp.concatenate(
        [local[sep_slab:, h * slab + sep_slab : (h + 1) * slab] for h in range(layers)], axis=1
    )
    shared_of = lambda m: jnp.concatenate(
        [m[:, h * outer_slab : h * outer_slab + shared_slab] for h in range(layers)], axis=1
    )
    own_shared = shared_of(direct_rows[:shared_slab]) - lax.dot_general(
        factor_own[:, :shared_slab], shared_of(joined[:, :outer_all]), (((0,), (0,)), ((), ())),
        precision=HIGHEST, preferred_element_type=jnp.float32,
    )
    cousin = partner(own_shared, "leaf", 1)
    product = lax.dot_general(
        factor_own, joined, (((0,), (0,)), ((), ())), precision=HIGHEST,
        preferred_element_type=jnp.float32,
    )
    with_own = direct_rows - product[:, :outer_all]
    with_sib = -product[:, outer_all:]
    merged = jnp.where(
        parity == 0,
        jnp.concatenate([with_own, with_sib], axis=1),
        jnp.concatenate([with_sib, with_own], axis=1),
    )
    cousin_sum = own_shared + cousin
    return (merged[None], cousin_sum[None])


def solution(mesh):
    placed = (P("leaf", "layer", None),)
    return jax.shard_map(
        condense,
        mesh=mesh,
        in_specs=placed,
        out_specs=(P("leaf", "layer", None), P("leaf", "layer", None)),
        check_vma=False,
    )
```

```python
import jax
import jax.numpy as jnp
from jax import lax
from jax.experimental import pallas as pl
from jax.experimental.pallas import tpu as pltpu
from jax.sharding import PartitionSpec as P


SEP = 512
SHARED = 512
BLOCK = 128
HIGHEST = lax.Precision.HIGHEST


def partner(value, axis, stride):
    mask = 2**stride
    pairs = [(source, source ^ mask) for source in range(lax.axis_size(axis))]
    return lax.ppermute(value, axis, pairs)


def gather_layer(value):
    layers = lax.axis_size("layer")
    pieces = [value]
    for shift in range(1, layers):
        pairs = [((dest + shift) % layers, dest) for dest in range(layers)]
        pieces.append(lax.ppermute(value, "layer", pairs))
    return jnp.concatenate(pieces, axis=0)


def _inv_factor_kernel(a_ref, x_ref, s_ref, w_ref):
    n = a_ref.shape[0]
    s_ref[...] = a_ref[...]
    rows_i = lax.broadcasted_iota(jnp.int32, (n, n), 0)
    cols_i = lax.broadcasted_iota(jnp.int32, (n, n), 1)
    w_ref[...] = jnp.where(rows_i == cols_i, 1.0, 0.0).astype(jnp.float32)
    x_ref[...] = jnp.zeros((n, n), jnp.float32)
    lane = lax.broadcasted_iota(jnp.int32, (1, n), 1)
    for grp in range(n // 8):
        r0 = grp * 8
        span = n - r0
        row_id = lax.broadcasted_iota(jnp.int32, (span, 1), 0) + r0

        def step(i, carry, r0=r0, span=span, row_id=row_id):
            j = r0 + i
            row_j = s_ref[pl.ds(j, 1), :]
            d = jnp.sum(jnp.where(lane == j, row_j, 0.0), axis=1, keepdims=True)
            scale = 1.0 / jnp.sqrt(d)
            l_row = jnp.where(lane >= j, row_j * scale, 0.0)
            x_row = w_ref[pl.ds(j, 1), :] * scale
            x_ref[pl.ds(j, 1), :] = x_row
            rows = s_ref[r0:, :]
            col = jnp.sum(jnp.where(lane == j, rows, 0.0), axis=1, keepdims=True)
            l_col = jnp.where(row_id > j, col * scale, 0.0)
            s_ref[r0:, :] = rows - l_col * l_row
            w_ref[r0:, :] = w_ref[r0:, :] - l_col * x_row
            return carry

        lax.fori_loop(0, 8, step, 0)


def inverse_factor(a):
    n = a.shape[0]
    return pl.pallas_call(
        _inv_factor_kernel,
        out_shape=jax.ShapeDtypeStruct((n, n), jnp.float32),
        in_specs=[pl.BlockSpec(memory_space=pltpu.VMEM)],
        out_specs=pl.BlockSpec(memory_space=pltpu.VMEM),
        scratch_shapes=[pltpu.VMEM((n, n), jnp.float32), pltpu.VMEM((n, n), jnp.float32)],
    )(a)


def mm(a, b):
    return jnp.dot(a, b, precision=HIGHEST, preferred_element_type=jnp.float32)


def mm_nt(a, b):
    return lax.dot_general(
        a, b, (((1,), (1,)), ((), ())), precision=HIGHEST, preferred_element_type=jnp.float32
    )


def blocked_cholesky(sepmat, first_diag):
    n = sepmat.shape[0]
    nb = n // BLOCK
    trailing = sepmat
    panels = []
    inverses = []
    for k in range(nb):
        diag = first_diag if k == 0 else trailing[:BLOCK, :BLOCK]
        inv = inverse_factor(diag)
        inverses.append(inv)
        if k + 1 < nb:
            below = trailing[BLOCK:, :BLOCK]
            panel = mm_nt(below, inv)
            panels.append(panel)
            trailing = trailing[BLOCK:, BLOCK:] - mm_nt(panel, panel)
    return panels, inverses


def forward_solve(panels, inverses, rhs):
    nb = len(inverses)
    out = []
    rest = rhs
    for k in range(nb):
        gk = mm(inverses[k], rest[:BLOCK])
        out.append(gk)
        if k + 1 < nb:
            rest = rest[BLOCK:] - mm(panels[k], gk)
    return jnp.concatenate(out, axis=0)


def condense(schur_blocks):
    layers = lax.axis_size("layer")
    local = schur_blocks[0]
    slab = local.shape[0]
    sep_slab = SEP // layers
    outer_slab = slab - sep_slab
    shared_slab = SHARED // layers
    outer_all = local.shape[1] - SEP
    me = lax.axis_index("layer")
    parity = lax.axis_index("leaf") % 2

    sep_rows = local[:sep_slab]
    sep_cols = jnp.concatenate(
        [sep_rows[:, h * slab : h * slab + sep_slab] for h in range(layers)], axis=1
    )
    out_cols = jnp.concatenate(
        [sep_rows[:, h * slab + sep_slab : (h + 1) * slab] for h in range(layers)], axis=1
    )
    sibling = partner(sep_cols, "leaf", 0)
    summed = sep_cols + sibling
    first_diag = lax.dynamic_slice_in_dim(summed, me * sep_slab, sep_slab, axis=1)
    rows_rel = gather_layer(summed)
    doubled = jnp.concatenate([rows_rel, rows_rel], axis=1)
    sepmat = lax.dynamic_slice_in_dim(doubled, me * sep_slab, SEP, axis=1)

    out_cols, sepmat = lax.optimization_barrier((out_cols, sepmat))
    coupling_own = gather_layer(out_cols)
    coupling_sib = partner(coupling_own, "leaf", 0)

    panels, inverses = blocked_cholesky(sepmat, first_diag)
    joined = forward_solve(panels, inverses, jnp.concatenate([coupling_own, coupling_sib], axis=1))
    factor_own = lax.dynamic_slice_in_dim(joined, me * outer_slab, outer_slab, axis=1)

    direct_rows = jnp.concatenate(
        [local[sep_slab:, h * slab + sep_slab : (h + 1) * slab] for h in range(layers)], axis=1
    )
    shared_of = lambda m: jnp.concatenate(
        [m[:, h * outer_slab : h * outer_slab + shared_slab] for h in range(layers)], axis=1
    )
    own_shared = shared_of(direct_rows[:shared_slab]) - lax.dot_general(
        factor_own[:, :shared_slab], shared_of(joined[:, :outer_all]), (((0,), (0,)), ((), ())),
        precision=HIGHEST, preferred_element_type=jnp.float32,
    )
    cousin = partner(own_shared, "leaf", 1)
    product = lax.dot_general(
        factor_own, joined, (((0,), (0,)), ((), ())), precision=HIGHEST,
        preferred_element_type=jnp.float32,
    )
    with_own = direct_rows - product[:, :outer_all]
    with_sib = -product[:, outer_all:]
    merged = jnp.where(
        parity == 0,
        jnp.concatenate([with_own, with_sib], axis=1),
        jnp.concatenate([with_sib, with_own], axis=1),
    )
    cousin_sum = own_shared + cousin
    return (merged[None], cousin_sum[None])


def solution(mesh):
    placed = (P("leaf", "layer", None),)
    return jax.shard_map(
        condense,
        mesh=mesh,
        in_specs=placed,
        out_specs=(P("leaf", "layer", None), P("leaf", "layer", None)),
        check_vma=False,
    )
```

```python
import jax
import jax.numpy as jnp
from jax import lax
from jax.experimental import pallas as pl
from jax.experimental.pallas import tpu as pltpu
from jax.sharding import PartitionSpec as P


SEP = 512
SHARED = 512
BLOCK = 128
HIGHEST = lax.Precision.HIGHEST


def partner(value, axis, stride):
    mask = 2**stride
    pairs = [(source, source ^ mask) for source in range(lax.axis_size(axis))]
    return lax.ppermute(value, axis, pairs)


def gather_layer(value):
    layers = lax.axis_size("layer")
    pieces = [value]
    for shift in range(1, layers):
        pairs = [((dest + shift) % layers, dest) for dest in range(layers)]
        pieces.append(lax.ppermute(value, "layer", pairs))
    return jnp.concatenate(pieces, axis=0)


def _inv_factor_kernel(a_ref, x_ref, s_ref, w_ref):
    n = a_ref.shape[0]
    s_ref[...] = a_ref[...]
    rows_i = lax.broadcasted_iota(jnp.int32, (n, n), 0)
    cols_i = lax.broadcasted_iota(jnp.int32, (n, n), 1)
    w_ref[...] = jnp.where(rows_i == cols_i, 1.0, 0.0).astype(jnp.float32)
    lane = lax.broadcasted_iota(jnp.int32, (8, n), 1)
    sub = lax.broadcasted_iota(jnp.int32, (8, n), 0)
    for grp in range(n // 8):
        r0 = grp * 8
        panel = s_ref[r0 : r0 + 8, :]
        wp = w_ref[r0 : r0 + 8, :]
        urows = jnp.zeros((8, n), jnp.float32)
        xrows = jnp.zeros((8, n), jnp.float32)
        for i in range(8):
            j = r0 + i
            row = jnp.broadcast_to(panel[i : i + 1, :], (8, n))
            d = jnp.sum(jnp.where(lane == j, row, 0.0), axis=1, keepdims=True)
            scale = 1.0 / jnp.sqrt(d)
            l_row = jnp.where(lane >= j, row * scale, 0.0)
            x_row = jnp.broadcast_to(wp[i : i + 1, :], (8, n)) * scale
            urows = jnp.where(sub == i, l_row, urows)
            xrows = jnp.where(sub == i, x_row, xrows)
            coef = jnp.sum(jnp.where(lane == r0 + sub, l_row, 0.0), axis=1, keepdims=True)
            coef = jnp.where(sub > i, coef, 0.0)
            panel = panel - coef * l_row
            wp = wp - coef * x_row
        x_ref[r0 : r0 + 8, :] = xrows
        if r0 + 8 < n:
            lo = r0 + 8
            ucols = jnp.transpose(urows)[lo:, :]
            both = jnp.concatenate([urows, xrows], axis=1)
            upd = jnp.dot(ucols, both, precision=HIGHEST, preferred_element_type=jnp.float32)
            s_ref[lo:, :] = s_ref[lo:, :] - upd[:, :n]
            w_ref[lo:, :] = w_ref[lo:, :] - upd[:, n:]


def inverse_factor(a):
    n = a.shape[0]
    return pl.pallas_call(
        _inv_factor_kernel,
        out_shape=jax.ShapeDtypeStruct((n, n), jnp.float32),
        in_specs=[pl.BlockSpec(memory_space=pltpu.VMEM)],
        out_specs=pl.BlockSpec(memory_space=pltpu.VMEM),
        scratch_shapes=[pltpu.VMEM((n, n), jnp.float32), pltpu.VMEM((n, n), jnp.float32)],
    )(a)


def mm(a, b):
    return jnp.dot(a, b, precision=HIGHEST, preferred_element_type=jnp.float32)


def mm_nt(a, b):
    return lax.dot_general(
        a, b, (((1,), (1,)), ((), ())), precision=HIGHEST, preferred_element_type=jnp.float32
    )


def blocked_cholesky(sepmat, first_diag):
    n = sepmat.shape[0]
    nb = n // BLOCK
    trailing = sepmat
    panels = []
    inverses = []
    for k in range(nb):
        diag = first_diag if k == 0 else trailing[:BLOCK, :BLOCK]
        inv = inverse_factor(diag)
        inverses.append(inv)
        if k + 1 < nb:
            below = trailing[BLOCK:, :BLOCK]
            panel = mm_nt(below, inv)
            panels.append(panel)
            trailing = trailing[BLOCK:, BLOCK:] - mm_nt(panel, panel)
    return panels, inverses


def forward_solve(panels, inverses, rhs):
    nb = len(inverses)
    out = []
    rest = rhs
    for k in range(nb):
        gk = mm(inverses[k], rest[:BLOCK])
        out.append(gk)
        if k + 1 < nb:
            rest = rest[BLOCK:] - mm(panels[k], gk)
    return jnp.concatenate(out, axis=0)


def condense(schur_blocks):
    layers = lax.axis_size("layer")
    local = schur_blocks[0]
    slab = local.shape[0]
    sep_slab = SEP // layers
    outer_slab = slab - sep_slab
    shared_slab = SHARED // layers
    outer_all = local.shape[1] - SEP
    me = lax.axis_index("layer")
    parity = lax.axis_index("leaf") % 2

    sep_rows = local[:sep_slab]
    sep_cols = jnp.concatenate(
        [sep_rows[:, h * slab : h * slab + sep_slab] for h in range(layers)], axis=1
    )
    out_cols = jnp.concatenate(
        [sep_rows[:, h * slab + sep_slab : (h + 1) * slab] for h in range(layers)], axis=1
    )
    sibling = partner(sep_cols, "leaf", 0)
    summed = sep_cols + sibling
    first_diag = lax.dynamic_slice_in_dim(summed, me * sep_slab, sep_slab, axis=1)
    rows_rel = gather_layer(summed)
    doubled = jnp.concatenate([rows_rel, rows_rel], axis=1)
    sepmat = lax.dynamic_slice_in_dim(doubled, me * sep_slab, SEP, axis=1)

    out_cols, sepmat = lax.optimization_barrier((out_cols, sepmat))
    coupling_own = gather_layer(out_cols)
    coupling_sib = partner(coupling_own, "leaf", 0)

    panels, inverses = blocked_cholesky(sepmat, first_diag)
    joined = forward_solve(panels, inverses, jnp.concatenate([coupling_own, coupling_sib], axis=1))
    factor_own = lax.dynamic_slice_in_dim(joined, me * outer_slab, outer_slab, axis=1)

    direct_rows = jnp.concatenate(
        [local[sep_slab:, h * slab + sep_slab : (h + 1) * slab] for h in range(layers)], axis=1
    )
    shared_of = lambda m: jnp.concatenate(
        [m[:, h * outer_slab : h * outer_slab + shared_slab] for h in range(layers)], axis=1
    )
    own_shared = shared_of(direct_rows[:shared_slab]) - lax.dot_general(
        factor_own[:, :shared_slab], shared_of(joined[:, :outer_all]), (((0,), (0,)), ((), ())),
        precision=HIGHEST, preferred_element_type=jnp.float32,
    )
    cousin = partner(own_shared, "leaf", 1)
    product = lax.dot_general(
        factor_own, joined, (((0,), (0,)), ((), ())), precision=HIGHEST,
        preferred_element_type=jnp.float32,
    )
    with_own = direct_rows - product[:, :outer_all]
    with_sib = -product[:, outer_all:]
    merged = jnp.where(
        parity == 0,
        jnp.concatenate([with_own, with_sib], axis=1),
        jnp.concatenate([with_sib, with_own], axis=1),
    )
    cousin_sum = own_shared + cousin
    return (merged[None], cousin_sum[None])


def solution(mesh):
    placed = (P("leaf", "layer", None),)
    return jax.shard_map(
        condense,
        mesh=mesh,
        in_specs=placed,
        out_specs=(P("leaf", "layer", None), P("leaf", "layer", None)),
        check_vma=False,
    )
```

```python
import jax
import jax.numpy as jnp
from jax import lax
from jax.experimental import pallas as pl
from jax.experimental.pallas import tpu as pltpu
from jax.sharding import PartitionSpec as P


SEP = 512
SHARED = 512
BLOCK = 128
HIGHEST = lax.Precision.HIGHEST


def partner(value, axis, stride):
    mask = 2**stride
    pairs = [(source, source ^ mask) for source in range(lax.axis_size(axis))]
    return lax.ppermute(value, axis, pairs)


def gather_layer(value):
    layers = lax.axis_size("layer")
    pieces = [value]
    for shift in range(1, layers):
        pairs = [((dest + shift) % layers, dest) for dest in range(layers)]
        pieces.append(lax.ppermute(value, "layer", pairs))
    return jnp.concatenate(pieces, axis=0)


def _inv_factor_kernel(a_ref, x_ref, s_ref, w_ref):
    n = a_ref.shape[0]
    s_ref[...] = a_ref[...]
    rows_i = lax.broadcasted_iota(jnp.int32, (n, n), 0)
    cols_i = lax.broadcasted_iota(jnp.int32, (n, n), 1)
    w_ref[...] = jnp.where(rows_i == cols_i, 1.0, 0.0).astype(jnp.float32)
    x_ref[...] = jnp.zeros((n, n), jnp.float32)
    lane = lax.broadcasted_iota(jnp.int32, (1, n), 1)
    for grp in range(n // 8):
        r0 = grp * 8
        span = n - r0
        row_id = lax.broadcasted_iota(jnp.int32, (span, 1), 0) + r0

        def step(i, carry, r0=r0, span=span, row_id=row_id):
            j = r0 + i
            row_j = s_ref[pl.ds(j, 1), :]
            d = jnp.sum(jnp.where(lane == j, row_j, 0.0), axis=1, keepdims=True)
            scale = 1.0 / jnp.sqrt(d)
            l_row = jnp.where(lane >= j, row_j * scale, 0.0)
            x_row = w_ref[pl.ds(j, 1), :] * scale
            x_ref[pl.ds(j, 1), :] = x_row
            rows = s_ref[r0:, :]
            col = jnp.transpose(jnp.broadcast_to(l_row, (n, n)))[r0:, :]
            l_col = jnp.where(row_id > j, col, 0.0)
            s_ref[r0:, :] = rows - l_col * l_row
            w_ref[r0:, :] = w_ref[r0:, :] - l_col * x_row
            return carry

        lax.fori_loop(0, 8, step, 0)


def inverse_factor(a):
    n = a.shape[0]
    return pl.pallas_call(
        _inv_factor_kernel,
        out_shape=jax.ShapeDtypeStruct((n, n), jnp.float32),
        in_specs=[pl.BlockSpec(memory_space=pltpu.VMEM)],
        out_specs=pl.BlockSpec(memory_space=pltpu.VMEM),
        scratch_shapes=[pltpu.VMEM((n, n), jnp.float32), pltpu.VMEM((n, n), jnp.float32)],
    )(a)


def mm(a, b):
    return jnp.dot(a, b, precision=HIGHEST, preferred_element_type=jnp.float32)


def mm_nt(a, b):
    return lax.dot_general(
        a, b, (((1,), (1,)), ((), ())), precision=HIGHEST, preferred_element_type=jnp.float32
    )


def blocked_cholesky(sepmat, first_diag):
    n = sepmat.shape[0]
    nb = n // BLOCK
    trailing = sepmat
    panels = []
    inverses = []
    for k in range(nb):
        diag = first_diag if k == 0 else trailing[:BLOCK, :BLOCK]
        inv = inverse_factor(diag)
        inverses.append(inv)
        if k + 1 < nb:
            below = trailing[BLOCK:, :BLOCK]
            panel = mm_nt(below, inv)
            panels.append(panel)
            trailing = trailing[BLOCK:, BLOCK:] - mm_nt(panel, panel)
    return panels, inverses


def forward_solve(panels, inverses, rhs):
    nb = len(inverses)
    out = []
    rest = rhs
    for k in range(nb):
        gk = mm(inverses[k], rest[:BLOCK])
        out.append(gk)
        if k + 1 < nb:
            rest = rest[BLOCK:] - mm(panels[k], gk)
    return jnp.concatenate(out, axis=0)


def condense(schur_blocks):
    layers = lax.axis_size("layer")
    local = schur_blocks[0]
    slab = local.shape[0]
    sep_slab = SEP // layers
    outer_slab = slab - sep_slab
    shared_slab = SHARED // layers
    me = lax.axis_index("layer")
    parity = lax.axis_index("leaf") % 2

    sep_rows = local[:sep_slab]
    sep_cols = jnp.concatenate(
        [sep_rows[:, h * slab : h * slab + sep_slab] for h in range(layers)], axis=1
    )
    out_cols = jnp.concatenate(
        [sep_rows[:, h * slab + sep_slab : (h + 1) * slab] for h in range(layers)], axis=1
    )
    sibling = partner(sep_cols, "leaf", 0)
    summed = sep_cols + sibling
    first_diag = lax.dynamic_slice_in_dim(summed, me * sep_slab, sep_slab, axis=1)
    rows_rel = gather_layer(summed)
    doubled = jnp.concatenate([rows_rel, rows_rel], axis=1)
    sepmat = lax.dynamic_slice_in_dim(doubled, me * sep_slab, SEP, axis=1)

    out_cols, sepmat = lax.optimization_barrier((out_cols, sepmat))
    coupling_own = gather_layer(out_cols)

    panels, inverses = blocked_cholesky(sepmat, first_diag)
    joined_own = forward_solve(panels, inverses, coupling_own)
    joined_sib = partner(joined_own, "leaf", 0)
    factor_own = lax.dynamic_slice_in_dim(joined_own, me * outer_slab, outer_slab, axis=1)

    direct_rows = jnp.concatenate(
        [local[sep_slab:, h * slab + sep_slab : (h + 1) * slab] for h in range(layers)], axis=1
    )
    contract = (((0,), (0,)), ((), ()))
    with_own = direct_rows - lax.dot_general(
        factor_own, joined_own, contract, precision=HIGHEST, preferred_element_type=jnp.float32
    )
    own_shared = jnp.concatenate(
        [with_own[:shared_slab, h * outer_slab : h * outer_slab + shared_slab] for h in range(layers)],
        axis=1,
    )
    cousin = partner(own_shared, "leaf", 1)
    with_sib = -lax.dot_general(
        factor_own, joined_sib, contract, precision=HIGHEST, preferred_element_type=jnp.float32
    )
    merged = jnp.where(
        parity == 0,
        jnp.concatenate([with_own, with_sib], axis=1),
        jnp.concatenate([with_sib, with_own], axis=1),
    )
    cousin_sum = own_shared + cousin
    return (merged[None], cousin_sum[None])


def solution(mesh):
    placed = (P("leaf", "layer", None),)
    return jax.shard_map(
        condense,
        mesh=mesh,
        in_specs=placed,
        out_specs=(P("leaf", "layer", None), P("leaf", "layer", None)),
        check_vma=False,
    )
```

```python
import jax
import jax.numpy as jnp
from jax import lax
from jax.experimental import pallas as pl
from jax.experimental.pallas import tpu as pltpu
from jax.sharding import PartitionSpec as P


SEP = 512
SHARED = 512
BLOCK = 128
HIGHEST = lax.Precision.HIGHEST


def partner(value, axis, stride):
    mask = 2**stride
    pairs = [(source, source ^ mask) for source in range(lax.axis_size(axis))]
    return lax.ppermute(value, axis, pairs)


def gather_layer(value):
    layers = lax.axis_size("layer")
    pieces = [value]
    for shift in range(1, layers):
        pairs = [((dest + shift) % layers, dest) for dest in range(layers)]
        pieces.append(lax.ppermute(value, "layer", pairs))
    return jnp.concatenate(pieces, axis=0)


def _inv_factor_kernel(a_ref, x_ref, s_ref, w_ref):
    n = a_ref.shape[0]
    s_ref[...] = a_ref[...]
    rows_i = lax.broadcasted_iota(jnp.int32, (n, n), 0)
    cols_i = lax.broadcasted_iota(jnp.int32, (n, n), 1)
    w_ref[...] = jnp.where(rows_i == cols_i, 1.0, 0.0).astype(jnp.float32)
    x_ref[...] = jnp.zeros((n, n), jnp.float32)
    lane = lax.broadcasted_iota(jnp.int32, (1, n), 1)
    for grp in range(n // 8):
        r0 = grp * 8
        span = n - r0
        row_id = lax.broadcasted_iota(jnp.int32, (span, 1), 0) + r0

        def step(i, carry, r0=r0, span=span, row_id=row_id):
            j = r0 + i
            row_j = s_ref[pl.ds(j, 1), :]
            d = jnp.sum(jnp.where(lane == j, row_j, 0.0), axis=1, keepdims=True)
            scale = 1.0 / jnp.sqrt(d)
            l_row = jnp.where(lane >= j, row_j * scale, 0.0)
            x_row = w_ref[pl.ds(j, 1), :] * scale
            x_ref[pl.ds(j, 1), :] = x_row
            rows = s_ref[r0:, :]
            col = jnp.sum(jnp.where(lane == j, rows, 0.0), axis=1, keepdims=True)
            l_col = jnp.where(row_id > j, col * scale, 0.0)
            s_ref[r0:, :] = rows - l_col * l_row
            w_ref[r0:, :] = w_ref[r0:, :] - l_col * x_row
            return carry

        lax.fori_loop(0, 8, step, 0, unroll=4)


def inverse_factor(a):
    n = BLOCK
    return pl.pallas_call(
        _inv_factor_kernel,
        out_shape=jax.ShapeDtypeStruct((n, n), jnp.float32),
        grid=(1,),
        in_specs=[pl.BlockSpec((n, n), lambda i: (0, 0))],
        out_specs=pl.BlockSpec((n, n), lambda i: (0, 0)),
        scratch_shapes=[pltpu.VMEM((n, n), jnp.float32), pltpu.VMEM((n, n), jnp.float32)],
    )(a)


def mm(a, b):
    return jnp.dot(a, b, precision=HIGHEST, preferred_element_type=jnp.float32)


def mm_nt(a, b):
    return lax.dot_general(
        a, b, (((1,), (1,)), ((), ())), precision=HIGHEST, preferred_element_type=jnp.float32
    )


def blocked_cholesky(sepmat, first_diag):
    n = sepmat.shape[0]
    nb = n // BLOCK
    trailing = sepmat
    panels = []
    inverses = []
    for k in range(nb):
        diag = first_diag if k == 0 else trailing
        inv = inverse_factor(diag)
        inverses.append(inv)
        if k + 1 < nb:
            below = trailing[BLOCK:, :BLOCK]
            panel = mm_nt(below, inv)
            panels.append(panel)
            trailing = trailing[BLOCK:, BLOCK:] - mm_nt(panel, panel)
    return panels, inverses


def forward_solve(panels, inverses, rhs):
    nb = len(inverses)
    out = []
    rest = rhs
    for k in range(nb):
        gk = mm(inverses[k], rest[:BLOCK])
        out.append(gk)
        if k + 1 < nb:
            rest = rest[BLOCK:] - mm(panels[k], gk)
    return jnp.concatenate(out, axis=0)


def condense(schur_blocks):
    layers = lax.axis_size("layer")
    local = schur_blocks[0]
    slab = local.shape[0]
    sep_slab = SEP // layers
    outer_slab = slab - sep_slab
    shared_slab = SHARED // layers
    me = lax.axis_index("layer")
    parity = lax.axis_index("leaf") % 2

    sep_rows = local[:sep_slab]
    sep_cols = jnp.concatenate(
        [sep_rows[:, h * slab : h * slab + sep_slab] for h in range(layers)], axis=1
    )
    out_cols = jnp.concatenate(
        [sep_rows[:, h * slab + sep_slab : (h + 1) * slab] for h in range(layers)], axis=1
    )
    sibling = partner(sep_cols, "leaf", 0)
    summed = sep_cols + sibling
    first_diag = lax.dynamic_slice_in_dim(summed, me * sep_slab, sep_slab, axis=1)
    rows_rel = gather_layer(summed)
    doubled = jnp.concatenate([rows_rel, rows_rel], axis=1)
    sepmat = lax.dynamic_slice_in_dim(doubled, me * sep_slab, SEP, axis=1)

    out_cols, sepmat = lax.optimization_barrier((out_cols, sepmat))
    coupling_own = gather_layer(out_cols)

    panels, inverses = blocked_cholesky(sepmat, first_diag)
    joined_own = forward_solve(panels, inverses, coupling_own)
    joined_sib = partner(joined_own, "leaf", 0)
    factor_own = lax.dynamic_slice_in_dim(joined_own, me * outer_slab, outer_slab, axis=1)

    direct_rows = jnp.concatenate(
        [local[sep_slab:, h * slab + sep_slab : (h + 1) * slab] for h in range(layers)], axis=1
    )
    contract = (((0,), (0,)), ((), ()))
    with_own = direct_rows - lax.dot_general(
        factor_own, joined_own, contract, precision=HIGHEST, preferred_element_type=jnp.float32
    )
    own_shared = jnp.concatenate(
        [with_own[:shared_slab, h * outer_slab : h * outer_slab + shared_slab] for h in range(layers)],
        axis=1,
    )
    cousin = partner(own_shared, "leaf", 1)
    with_sib = -lax.dot_general(
        factor_own, joined_sib, contract, precision=HIGHEST, preferred_element_type=jnp.float32
    )
    merged = jnp.where(
        parity == 0,
        jnp.concatenate([with_own, with_sib], axis=1),
        jnp.concatenate([with_sib, with_own], axis=1),
    )
    cousin_sum = own_shared + cousin
    return (merged[None], cousin_sum[None])


def solution(mesh):
    placed = (P("leaf", "layer", None),)
    return jax.shard_map(
        condense,
        mesh=mesh,
        in_specs=placed,
        out_specs=(P("leaf", "layer", None), P("leaf", "layer", None)),
        check_vma=False,
    )
```

```python
import jax
import jax.numpy as jnp
from jax import lax
from jax.experimental import pallas as pl
from jax.experimental.pallas import tpu as pltpu
from jax.sharding import PartitionSpec as P


SEP = 512
SHARED = 512
BLOCK = 128
HIGHEST = lax.Precision.HIGHEST


def partner(value, axis, stride):
    mask = 2**stride
    pairs = [(source, source ^ mask) for source in range(lax.axis_size(axis))]
    return lax.ppermute(value, axis, pairs)


def gather_layer(value):
    layers = lax.axis_size("layer")
    pieces = [value]
    for shift in range(1, layers):
        pairs = [((dest + shift) % layers, dest) for dest in range(layers)]
        pieces.append(lax.ppermute(value, "layer", pairs))
    return jnp.concatenate(pieces, axis=0)


def _inv_factor_kernel(a_ref, x_ref, s_ref, w_ref):
    n = a_ref.shape[0]
    s_ref[...] = a_ref[...]
    rows_i = lax.broadcasted_iota(jnp.int32, (n, n), 0)
    cols_i = lax.broadcasted_iota(jnp.int32, (n, n), 1)
    w_ref[...] = jnp.where(rows_i == cols_i, 1.0, 0.0).astype(jnp.float32)
    x_ref[...] = jnp.zeros((n, n), jnp.float32)
    lane = lax.broadcasted_iota(jnp.int32, (1, n), 1)
    for grp in range(n // 8):
        r0 = grp * 8
        span = n - r0
        row_id = lax.broadcasted_iota(jnp.int32, (span, 1), 0) + r0

        def step(i, carry, r0=r0, span=span, row_id=row_id):
            j = r0 + i
            row_j = s_ref[pl.ds(j, 1), :]
            d = jnp.sum(jnp.where(lane == j, row_j, 0.0), axis=1, keepdims=True)
            scale = lax.rsqrt(d)
            l_row = jnp.where(lane >= j, row_j * scale, 0.0)
            x_row = w_ref[pl.ds(j, 1), :] * scale
            x_ref[pl.ds(j, 1), :] = x_row
            rows = s_ref[r0:, :]
            col = jnp.sum(jnp.where(lane == j, rows, 0.0), axis=1, keepdims=True)
            l_col = jnp.where(row_id > j, col * scale, 0.0)
            s_ref[r0:, :] = rows - l_col * l_row
            w_ref[r0:, :] = w_ref[r0:, :] - l_col * x_row
            return carry

        lax.fori_loop(0, 8, step, 0, unroll=4)


def inverse_factor(a):
    n = a.shape[0]
    return pl.pallas_call(
        _inv_factor_kernel,
        out_shape=jax.ShapeDtypeStruct((n, n), jnp.float32),
        in_specs=[pl.BlockSpec(memory_space=pltpu.VMEM)],
        out_specs=pl.BlockSpec(memory_space=pltpu.VMEM),
        scratch_shapes=[pltpu.VMEM((n, n), jnp.float32), pltpu.VMEM((n, n), jnp.float32)],
    )(a)


def mm(a, b):
    return jnp.dot(a, b, precision=HIGHEST, preferred_element_type=jnp.float32)


def mm_nt(a, b):
    return lax.dot_general(
        a, b, (((1,), (1,)), ((), ())), precision=HIGHEST, preferred_element_type=jnp.float32
    )


def blocked_cholesky(sepmat, first_diag):
    n = sepmat.shape[0]
    nb = n // BLOCK
    trailing = sepmat
    panels = []
    inverses = []
    for k in range(nb):
        diag = first_diag if k == 0 else trailing[:BLOCK, :BLOCK]
        inv = inverse_factor(diag)
        inverses.append(inv)
        if k + 1 < nb:
            below = trailing[BLOCK:, :BLOCK]
            panel = mm_nt(below, inv)
            panels.append(panel)
            trailing = trailing[BLOCK:, BLOCK:] - mm_nt(panel, panel)
    return panels, inverses


def forward_solve(panels, inverses, rhs):
    nb = len(inverses)
    out = []
    rest = rhs
    for k in range(nb):
        gk = mm(inverses[k], rest[:BLOCK])
        out.append(gk)
        if k + 1 < nb:
            rest = rest[BLOCK:] - mm(panels[k], gk)
    return jnp.concatenate(out, axis=0)


def condense(schur_blocks):
    layers = lax.axis_size("layer")
    local = schur_blocks[0]
    slab = local.shape[0]
    sep_slab = SEP // layers
    outer_slab = slab - sep_slab
    shared_slab = SHARED // layers
    me = lax.axis_index("layer")
    parity = lax.axis_index("leaf") % 2

    sep_rows = local[:sep_slab]
    sep_cols = jnp.concatenate(
        [sep_rows[:, h * slab : h * slab + sep_slab] for h in range(layers)], axis=1
    )
    out_cols = jnp.concatenate(
        [sep_rows[:, h * slab + sep_slab : (h + 1) * slab] for h in range(layers)], axis=1
    )
    sibling = partner(sep_cols, "leaf", 0)
    summed = sep_cols + sibling
    first_diag = lax.dynamic_slice_in_dim(summed, me * sep_slab, sep_slab, axis=1)
    rows_rel = gather_layer(summed)
    doubled = jnp.concatenate([rows_rel, rows_rel], axis=1)
    sepmat = lax.dynamic_slice_in_dim(doubled, me * sep_slab, SEP, axis=1)

    out_cols, sepmat = lax.optimization_barrier((out_cols, sepmat))
    coupling_own = gather_layer(out_cols)

    panels, inverses = blocked_cholesky(sepmat, first_diag)
    joined_own = forward_solve(panels, inverses, coupling_own)
    joined_sib = partner(joined_own, "leaf", 0)
    factor_own = lax.dynamic_slice_in_dim(joined_own, me * outer_slab, outer_slab, axis=1)

    direct_rows = jnp.concatenate(
        [local[sep_slab:, h * slab + sep_slab : (h + 1) * slab] for h in range(layers)], axis=1
    )
    contract = (((0,), (0,)), ((), ()))
    with_own = direct_rows - lax.dot_general(
        factor_own, joined_own, contract, precision=HIGHEST, preferred_element_type=jnp.float32
    )
    own_shared = jnp.concatenate(
        [with_own[:shared_slab, h * outer_slab : h * outer_slab + shared_slab] for h in range(layers)],
        axis=1,
    )
    cousin = partner(own_shared, "leaf", 1)
    with_sib = -lax.dot_general(
        factor_own, joined_sib, contract, precision=HIGHEST, preferred_element_type=jnp.float32
    )
    merged = jnp.where(
        parity == 0,
        jnp.concatenate([with_own, with_sib], axis=1),
        jnp.concatenate([with_sib, with_own], axis=1),
    )
    cousin_sum = own_shared + cousin
    return (merged[None], cousin_sum[None])


def solution(mesh):
    placed = (P("leaf", "layer", None),)
    return jax.shard_map(
        condense,
        mesh=mesh,
        in_specs=placed,
        out_specs=(P("leaf", "layer", None), P("leaf", "layer", None)),
        check_vma=False,
    )
```
